32 devices in a mesh: groups: 2 (over y), user: 8 (over z, x), item: 2 (over core).
Axes of the slice: x: 2, y: 2, z: 4, core: 2. Of those that a mesh axis runs over, the one named last changes fastest.
Arguments:
- user_factors: float32 [49152, 256], P(('groups', 'user')), parts along dimension 0, may hold values from -1.5 to 1.5
- item_factors: float32 [16384, 256], P(('groups', 'user', 'item')), parts along dimension 0, may hold values from -1.5 to 1.5
- stratum_masks: int32 [4], P('groups'), parts along dimension 0, may hold values from 1 to 7
- block_codes: int32 [16, 2, 128], P(('groups', 'user'), 'item'), parts along dimension 0, may hold values from 0 to 95, as said below
- block_counts: int32 [16, 2, 2], P(('groups', 'user'), 'item'), parts along dimension 0, may hold values from 1 to 64
- ratings: bfloat16 [16, 2, 128, 128, 128], P(('groups', 'user'), 'item'), parts along dimension 0, may hold values from -6 to 6
Outputs:
- user_out: float32 [49152, 256], P(('groups', 'user')), parts along dimension 0
- item_out: float32 [16384, 256], P(('groups', 'user', 'item')), parts along dimension 0
The draws below stay inside these ranges and needn't reach their ends.
There are 2 independent parts, one for each index of `groups`. The reference program is written for one: setup_inputs(seed, part) draws one part's arguments, and reference() takes and returns one part's arrays. A program takes and returns all parts, laid end to end along the dimension named above; each array names one. Nothing has to cross between parts.
Inputs may be any that keep to these rules, and one draw needn't show every extreme that they name: `stratum_masks`: each mask m pairs user index u with user index u XOR m. `block_codes`: within one device and stratum the 64 codes are distinct.
All inputs are finite; a program needn't handle non-finite values.
Results may differ from the reference program's by a relative error of at most 0.0011.
Values sent between devices are 32-bit elements; how exact they have to be, the bound alone decides.
No kernel may reach another device: no remote copies, remote signals or barrier semaphores. Data moves between devices by JAX's collectives and lax.ppermute only.
A program may use at most 128 MiB of HBM per device.

```python
import jax
import jax.numpy as jnp
from jax import lax

R = 256
TILE = 128
USER_DEV = 3072
ITEM_DEV = 512
CAP = 64
STRATA = 2
USERS = 24576
ITEMS = 8192
N_USER = 8
N_ITEM = 2


def draw_block_codes(key, part):
    code_count = USER_DEV // TILE * (ITEM_DEV // TILE)
    keys = jax.random.split(jax.random.fold_in(key, 11), N_USER * N_ITEM * STRATA)
    picked = jax.vmap(lambda one_key: jax.random.permutation(one_key, code_count)[:CAP])(keys)
    return picked.reshape(N_USER, N_ITEM, STRATA * CAP).astype(jnp.int32)


def draw_block_counts(key, part):
    first_key, second_key, third_key = jax.random.split(jax.random.fold_in(key, 23), 3)
    shape_all = (N_USER, N_ITEM, STRATA)
    lower = jax.random.randint(first_key, shape_all, 1, max(CAP // 4, 1) + 1)
    factor = jax.random.randint(second_key, shape_all, 1, 5)
    counts = jnp.minimum(lower * factor, CAP)
    chosen = jax.random.randint(third_key, (STRATA,), 0, N_USER * N_ITEM)
    device_index = jnp.arange(N_USER * N_ITEM, dtype=jnp.int32).reshape(N_USER, N_ITEM)
    filled = device_index[:, :, None] == chosen[None, None, :]
    return jnp.where(filled, CAP, counts).astype(jnp.int32)


def shard_levels(key, shape, cuts, smallest, largest):
    level = 1.0
    for dim, parts in cuts:
        heights = jax.random.uniform(jax.random.fold_in(jax.random.fold_in(key, 6), dim), (parts,), jnp.float32, smallest / len(cuts), largest / len(cuts))
        level = level * jnp.repeat(jnp.exp(heights), shape[dim] // parts).reshape((-1,) + (1,) * (len(shape) - 1 - dim))
    return level


def gaussian(own_key, shape, width, most, cuts=(), kind=jnp.bfloat16):
    array = width * jax.random.normal(own_key, shape, jnp.float32)
    if cuts:
        array = array * shard_levels(own_key, shape, cuts, -0.22, 0.18)
    return jnp.clip(array, -most, most).astype(kind)


def setup_inputs(seed: int = 0, part: int = 0) -> dict:
    key_list = jax.random.split(jax.random.key(seed), 7)
    part_splits = jax.random.split(jax.random.fold_in(key_list[6], part), 7)
    user_factors = gaussian(part_splits[0], (USERS, R), 0.25, 1.5, ((0, 8),), jnp.float32)
    item_factors = gaussian(part_splits[1], (ITEMS, R), 0.25, 1.5, ((0, 16),), jnp.float32)
    stratum_masks = jax.random.randint(part_splits[2], (STRATA,), 1, N_USER).astype(jnp.int32)
    block_codes = draw_block_codes(jax.random.fold_in(jax.random.fold_in(key_list[6], part), 71), part)
    block_counts = draw_block_counts(jax.random.fold_in(jax.random.fold_in(key_list[6], part), 71), part)
    ratings = gaussian(part_splits[5], (N_USER, N_ITEM, STRATA * CAP, TILE, TILE), 1.0, 6.0, ((0, 8), (1, 2)))
    return dict(user_factors=user_factors, item_factors=item_factors, stratum_masks=stratum_masks, block_codes=block_codes, block_counts=block_counts, ratings=ratings)


LEARNING_RATE = 0.02
WEIGHT_DECAY = 0.1


def device_grads(user_tiles, panel, codes, count, blocks):
    user_bf = user_tiles.astype(jnp.bfloat16)
    panel_bf = panel.astype(jnp.bfloat16)
    item_count = panel.shape[0]
    user_count = user_tiles.shape[0]
    tile_user = (codes // item_count).astype(jnp.int32)
    tile_item = (codes % item_count).astype(jnp.int32)
    user_sel = jnp.take(user_bf, tile_user, axis=0).astype(jnp.float32)
    item_sel = jnp.take(panel_bf, tile_item, axis=0).astype(jnp.float32)
    scores = jnp.einsum("kar,kbr->kab", user_sel, item_sel)
    live = (jnp.arange(codes.shape[0], dtype=jnp.int32) < count).astype(jnp.float32)
    errors = ((scores - blocks.astype(jnp.float32)) * live[:, None, None]).astype(jnp.bfloat16).astype(jnp.float32)
    grad_user_each = jnp.einsum("kab,kbr->kar", errors, item_sel)
    grad_item_each = jnp.einsum("kab,kar->kbr", errors, user_sel)
    one_user = (tile_user[:, None] == jnp.arange(user_count, dtype=jnp.int32)[None, :]).astype(jnp.float32)
    one_item = (tile_item[:, None] == jnp.arange(item_count, dtype=jnp.int32)[None, :]).astype(jnp.float32)
    grad_user = jnp.einsum("kt,kar->tar", one_user, grad_user_each, precision=lax.Precision.HIGHEST)
    grad_item = jnp.einsum("kt,kar->tar", one_item, grad_item_each, precision=lax.Precision.HIGHEST)
    return grad_user, grad_item


def reference(user_factors, item_factors, stratum_masks, block_codes, block_counts, ratings):
    user_tiles = USER_DEV // TILE
    item_tiles = ITEM_DEV // TILE
    user_rows = user_factors.reshape(N_USER, user_tiles, TILE, R)
    item_rows = item_factors.reshape(N_USER, N_ITEM, item_tiles, TILE, R)
    for stratum in range(STRATA):
        stratum_mask = stratum_masks[stratum]
        partner = jnp.bitwise_xor(jnp.arange(N_USER, dtype=jnp.int32), stratum_mask.astype(jnp.int32))
        panels = jnp.take(item_rows, partner, axis=0)
        codes = block_codes[:, :, stratum * CAP:(stratum + 1) * CAP]
        counts = block_counts[:, :, stratum]
        blocks = ratings[:, :, stratum * CAP:(stratum + 1) * CAP]

        def one_block(packed):
            user_here, panel_here, code_here, count_here, block_here = packed
            grad_user = jnp.zeros((user_tiles, TILE, R), jnp.float32)
            grad_items = []
            for column in range(N_ITEM):
                part_user, part_item = device_grads(user_here, panel_here[column], code_here[column], count_here[column], block_here[column])
                grad_user = grad_user + part_user
                grad_items.append(part_item)
            return grad_user, jnp.stack(grad_items)

        grad_user, grad_item = lax.map(one_block, (user_rows, panels, codes, counts, blocks))
        user_rows = user_rows - LEARNING_RATE * (grad_user + WEIGHT_DECAY * user_rows)
        panels_new = panels - LEARNING_RATE * (grad_item + WEIGHT_DECAY * panels)
        item_rows = jnp.take(panels_new, partner, axis=0)
    return user_rows.reshape(USER_DEV * N_USER, R), item_rows.reshape(ITEM_DEV * N_USER * N_ITEM, R)
```

```python
import jax
import jax.numpy as jnp
from jax import lax
from jax.sharding import PartitionSpec as P

LEARNING_RATE = 0.02
WEIGHT_DECAY = 0.1


def moved(value, partner_mask):
    count = lax.axis_size("user")

    def branch(mask):
        if mask == 0:
            return lambda held: held
        pairs = [(source, source ^ mask) for source in range(count)]
        return lambda held: lax.ppermute(held, "user", pairs)

    return lax.switch(partner_mask, [branch(mask) for mask in range(count)], value)


def item_sum(value):
    if lax.axis_size("item") == 2:
        return value + lax.ppermute(value, "item", [(0, 1), (1, 0)])
    return lax.psum(value, "item")


def local_grads(user_rows, panel_rows, codes, count, blocks):
    tile_size = blocks.shape[-1]
    user_tiles = user_rows.shape[0] // tile_size
    item_tiles = panel_rows.shape[0] // tile_size
    code_count = user_tiles * item_tiles
    slot_count = codes.shape[0]
    user_bf = user_rows.astype(jnp.bfloat16)
    panel_bf = panel_rows.astype(jnp.bfloat16)
    hits = (codes[:, None] == lax.iota(jnp.int32, code_count)[None, :]) & (
        lax.iota(jnp.int32, slot_count) < count
    )[:, None]
    live = jnp.any(hits, axis=0)
    slot_of = jnp.sum(jnp.where(hits, lax.iota(jnp.int32, slot_count)[:, None], 0), axis=0)
    dense = jnp.take(blocks, slot_of, axis=0).reshape(user_tiles, item_tiles, tile_size, tile_size)
    dense = dense.transpose(0, 2, 1, 3).reshape(user_tiles * tile_size, item_tiles * tile_size)
    live_dense = jnp.broadcast_to(
        live.reshape(user_tiles, 1, item_tiles, 1).astype(jnp.float32),
        (user_tiles, tile_size, item_tiles, tile_size),
    ).reshape(user_tiles * tile_size, item_tiles * tile_size)
    scores = lax.dot_general(
        user_bf, panel_bf, (((1,), (1,)), ((), ())), preferred_element_type=jnp.float32
    )
    errors = ((scores - dense.astype(jnp.float32)) * live_dense).astype(jnp.bfloat16)
    grad_user = lax.dot_general(
        errors, panel_bf, (((1,), (0,)), ((), ())), preferred_element_type=jnp.float32
    )
    grad_panel = lax.dot_general(
        errors, user_bf, (((0,), (0,)), ((), ())), preferred_element_type=jnp.float32
    )
    return grad_user, grad_panel


def local(user_factors, item_factors, stratum_masks, block_codes, block_counts, ratings):
    stratum_total = stratum_masks.shape[0]
    slot_count = block_codes.shape[-1] // stratum_total

    user_rows = user_factors
    panel_now = moved(item_factors, stratum_masks[0])
    for stratum in range(stratum_total):
        codes = block_codes[0, 0, stratum * slot_count : (stratum + 1) * slot_count]
        count = block_counts[0, 0, stratum]
        blocks = ratings[0, 0, stratum * slot_count : (stratum + 1) * slot_count]
        grad_user, grad_panel = local_grads(user_rows, panel_now, codes, count, blocks)
        panel_next = panel_now - LEARNING_RATE * (grad_panel + WEIGHT_DECAY * panel_now)
        if stratum + 1 < stratum_total:
            step_mask = jnp.bitwise_xor(stratum_masks[stratum], stratum_masks[stratum + 1])
        else:
            step_mask = stratum_masks[stratum]
        panel_now = moved(panel_next, step_mask)
        grad_total = item_sum(grad_user)
        user_rows = user_rows - LEARNING_RATE * (grad_total + WEIGHT_DECAY * user_rows)
    return (user_rows, panel_now)


def solution(mesh):
    placed = (
        P(("groups", "user"), None),
        P(("groups", "user", "item"), None),
        P("groups"),
        P(("groups", "user"), "item", None),
        P(("groups", "user"), "item", None),
        P(("groups", "user"), "item", None, None, None),
    )
    return jax.shard_map(
        local,
        mesh=mesh,
        in_specs=placed,
        out_specs=(P(("groups", "user"), None), P(("groups", "user", "item"), None)),
        check_vma=False,
    )
```

```python
import functools

import jax
import jax.numpy as jnp
from jax import lax
from jax.experimental import pallas as pl
from jax.experimental.pallas import tpu as pltpu
from jax.sharding import PartitionSpec as P

LEARNING_RATE = 0.02
WEIGHT_DECAY = 0.1
TILES_PER_STEP = 2


def moved(value, partner_mask):
    count = lax.axis_size("user")

    def branch(mask):
        if mask == 0:
            return lambda held: held
        pairs = [(source, source ^ mask) for source in range(count)]
        return lambda held: lax.ppermute(held, "user", pairs)

    return lax.switch(partner_mask, [branch(mask) for mask in range(count)], value)


def item_sum(value):
    if lax.axis_size("item") == 2:
        return value + lax.ppermute(value, "item", [(0, 1), (1, 0)])
    return lax.psum(value, "item")


def grads_kernel(item_tiles, slot_ref, live_ref, user_ref, panel_ref, *rest):
    block_refs = rest[: TILES_PER_STEP * item_tiles]
    grad_user_ref, grad_panel_ref = rest[TILES_PER_STEP * item_tiles :]
    step = pl.program_id(0)
    tile_size = block_refs[0].shape[-1]

    @pl.when(step == 0)
    def _():
        grad_panel_ref[...] = jnp.zeros_like(grad_panel_ref)

    for inner in range(TILES_PER_STEP):
        rows = pl.ds(inner * tile_size, tile_size)
        user_bf = user_ref[rows, :].astype(jnp.bfloat16)
        grad_user = None
        for column in range(item_tiles):
            code = (step * TILES_PER_STEP + inner) * item_tiles + column
            live = live_ref[code].astype(jnp.float32)
            panel_bf = panel_ref[pl.ds(column * tile_size, tile_size), :]
            scores = lax.dot_general(
                user_bf, panel_bf, (((1,), (1,)), ((), ())), preferred_element_type=jnp.float32
            )
            block = block_refs[inner * item_tiles + column][...].astype(jnp.float32)
            errors = ((scores - block) * live).astype(jnp.bfloat16)
            part = lax.dot_general(
                errors, panel_bf, (((1,), (0,)), ((), ())), preferred_element_type=jnp.float32
            )
            grad_user = part if grad_user is None else grad_user + part
            cols = pl.ds(column * tile_size, tile_size)
            grad_panel_ref[cols, :] += lax.dot_general(
                errors, user_bf, (((0,), (0,)), ((), ())), preferred_element_type=jnp.float32
            )
        grad_user_ref[rows, :] = grad_user


def local_grads(user_rows, panel_bf, codes, count, blocks, first):
    tile_size = blocks.shape[-1]
    rank = user_rows.shape[1]
    user_tiles = user_rows.shape[0] // tile_size
    item_tiles = panel_bf.shape[0] // tile_size
    code_count = user_tiles * item_tiles
    slot_count = codes.shape[0]
    hits = (codes[:, None] == lax.iota(jnp.int32, code_count)[None, :]) & (
        lax.iota(jnp.int32, slot_count) < count
    )[:, None]
    live = jnp.any(hits, axis=0).astype(jnp.int32)
    slot_of = first + jnp.sum(jnp.where(hits, lax.iota(jnp.int32, slot_count)[:, None], 0), axis=0)

    def block_spec(inner, column):
        def index(step, slot_ref, live_ref):
            return (slot_ref[(step * TILES_PER_STEP + inner) * item_tiles + column], 0, 0)

        return pl.BlockSpec((None, tile_size, tile_size), index)

    rows = TILES_PER_STEP * tile_size
    grid_spec = pltpu.PrefetchScalarGridSpec(
        num_scalar_prefetch=2,
        grid=(user_tiles // TILES_PER_STEP,),
        in_specs=[
            pl.BlockSpec((rows, rank), lambda step, slot_ref, live_ref: (step, 0)),
            pl.BlockSpec((item_tiles * tile_size, rank), lambda step, slot_ref, live_ref: (0, 0)),
        ]
        + [block_spec(inner, column) for inner in range(TILES_PER_STEP) for column in range(item_tiles)],
        out_specs=[
            pl.BlockSpec((rows, rank), lambda step, slot_ref, live_ref: (step, 0)),
            pl.BlockSpec((item_tiles * tile_size, rank), lambda step, slot_ref, live_ref: (0, 0)),
        ],
    )
    flops = 3 * 2 * code_count * tile_size * tile_size * rank
    moved_bytes = user_rows.size * 4 * 2 + panel_bf.size * 2 + code_count * tile_size * tile_size * 2 + panel_bf.size * 4
    return pl.pallas_call(
        functools.partial(grads_kernel, item_tiles),
        grid_spec=grid_spec,
        out_shape=[
            jax.ShapeDtypeStruct(user_rows.shape, jnp.float32),
            jax.ShapeDtypeStruct(panel_bf.shape, jnp.float32),
        ],
        compiler_params=pltpu.CompilerParams(dimension_semantics=("arbitrary",)),
        cost_estimate=pl.CostEstimate(flops=flops, bytes_accessed=moved_bytes, transcendentals=0),
    )(slot_of, live, user_rows, panel_bf, *([blocks] * (TILES_PER_STEP * item_tiles)))


def local(user_factors, item_factors, stratum_masks, block_codes, block_counts, ratings):
    stratum_total = stratum_masks.shape[0]
    slot_count = block_codes.shape[-1] // stratum_total
    tile_size = ratings.shape[-1]
    all_blocks = ratings.reshape(-1, tile_size, tile_size)

    user_rows = user_factors
    panel_now = moved(item_factors, stratum_masks[0])
    for stratum in range(stratum_total):
        codes = block_codes[0, 0, stratum * slot_count : (stratum + 1) * slot_count]
        count = block_counts[0, 0, stratum]
        grad_user, grad_panel = local_grads(
            user_rows, panel_now.astype(jnp.bfloat16), codes, count, all_blocks, stratum * slot_count
        )
        panel_next = panel_now - LEARNING_RATE * (grad_panel + WEIGHT_DECAY * panel_now)
        if stratum + 1 < stratum_total:
            step_mask = jnp.bitwise_xor(stratum_masks[stratum], stratum_masks[stratum + 1])
        else:
            step_mask = stratum_masks[stratum]
        panel_now = moved(panel_next, step_mask)
        grad_total = item_sum(grad_user)
        user_rows = user_rows - LEARNING_RATE * (grad_total + WEIGHT_DECAY * user_rows)
    return (user_rows, panel_now)


def solution(mesh):
    placed = (
        P(("groups", "user"), None),
        P(("groups", "user", "item"), None),
        P("groups"),
        P(("groups", "user"), "item", None),
        P(("groups", "user"), "item", None),
        P(("groups", "user"), "item", None, None, None),
    )
    return jax.shard_map(
        local,
        mesh=mesh,
        in_specs=placed,
        out_specs=(P(("groups", "user"), None), P(("groups", "user", "item"), None)),
        check_vma=False,
    )
```

```python
import functools

import jax
import jax.numpy as jnp
from jax import lax
from jax.experimental import pallas as pl
from jax.experimental.pallas import tpu as pltpu
from jax.sharding import PartitionSpec as P

LEARNING_RATE = 0.02
WEIGHT_DECAY = 0.1
TILES_PER_STEP = 4


def moved(value, partner_mask):
    count = lax.axis_size("user")

    def branch(mask):
        if mask == 0:
            return lambda held: held
        pairs = [(source, source ^ mask) for source in range(count)]
        return lambda held: lax.ppermute(held, "user", pairs)

    return lax.switch(partner_mask, [branch(mask) for mask in range(count)], value)


def item_sum(value):
    if lax.axis_size("item") == 2:
        return value + lax.ppermute(value, "item", [(0, 1), (1, 0)])
    return lax.psum(value, "item")


def grads_kernel(item_tiles, slot_ref, live_ref, user_ref, user_t_ref, panel_ref, panel_t_ref, *rest):
    block_refs = rest[: TILES_PER_STEP * item_tiles]
    grad_user_ref, grad_panel_t_ref = rest[TILES_PER_STEP * item_tiles :]
    step = pl.program_id(0)
    tile_size = block_refs[0].shape[-1]

    @pl.when(step == 0)
    def _():
        grad_panel_t_ref[...] = jnp.zeros_like(grad_panel_t_ref)

    scores = jnp.dot(user_ref[...], panel_t_ref[...], preferred_element_type=jnp.float32)
    pieces = []
    for inner in range(TILES_PER_STEP):
        row = []
        for column in range(item_tiles):
            code = (step * TILES_PER_STEP + inner) * item_tiles + column
            live = live_ref[code].astype(jnp.float32)
            block = block_refs[inner * item_tiles + column][...].astype(jnp.float32)
            part = scores[inner * tile_size : (inner + 1) * tile_size, column * tile_size : (column + 1) * tile_size]
            row.append(((part - block) * live).astype(jnp.bfloat16))
        pieces.append(jnp.concatenate(row, axis=1))
    errors = jnp.concatenate(pieces, axis=0)
    grad_user_ref[...] = jnp.dot(errors, panel_ref[...], preferred_element_type=jnp.float32)
    grad_panel_t_ref[...] += jnp.dot(user_t_ref[...], errors, preferred_element_type=jnp.float32)


def local_grads(user_bf, user_t, panel_bf, panel_t, codes, count, blocks, first):
    tile_size = blocks.shape[-1]
    rank = user_bf.shape[1]
    user_tiles = user_bf.shape[0] // tile_size
    item_tiles = panel_bf.shape[0] // tile_size
    code_count = user_tiles * item_tiles
    slot_count = codes.shape[0]
    hits = (codes[:, None] == lax.iota(jnp.int32, code_count)[None, :]) & (
        lax.iota(jnp.int32, slot_count) < count
    )[:, None]
    live = jnp.any(hits, axis=0).astype(jnp.int32)
    slot_of = first + jnp.sum(jnp.where(hits, lax.iota(jnp.int32, slot_count)[:, None], 0), axis=0)

    def block_spec(inner, column):
        def index(step, slot_ref, live_ref):
            return (slot_ref[(step * TILES_PER_STEP + inner) * item_tiles + column], 0, 0)

        return pl.BlockSpec((None, tile_size, tile_size), index)

    rows = TILES_PER_STEP * tile_size
    columns = item_tiles * tile_size
    grid_spec = pltpu.PrefetchScalarGridSpec(
        num_scalar_prefetch=2,
        grid=(user_tiles // TILES_PER_STEP,),
        in_specs=[
            pl.BlockSpec((rows, rank), lambda step, slot_ref, live_ref: (step, 0)),
            pl.BlockSpec((rank, rows), lambda step, slot_ref, live_ref: (0, step)),
            pl.BlockSpec((columns, rank), lambda step, slot_ref, live_ref: (0, 0)),
            pl.BlockSpec((rank, columns), lambda step, slot_ref, live_ref: (0, 0)),
        ]
        + [block_spec(inner, column) for inner in range(TILES_PER_STEP) for column in range(item_tiles)],
        out_specs=[
            pl.BlockSpec((rows, rank), lambda step, slot_ref, live_ref: (step, 0)),
            pl.BlockSpec((rank, columns), lambda step, slot_ref, live_ref: (0, 0)),
        ],
    )
    flops = 3 * 2 * code_count * tile_size * tile_size * rank
    moved_bytes = user_bf.size * 2 * 2 + user_bf.size * 4 + panel_bf.size * 8 + code_count * tile_size * tile_size * 2
    return pl.pallas_call(
        functools.partial(grads_kernel, item_tiles),
        grid_spec=grid_spec,
        out_shape=[
            jax.ShapeDtypeStruct(user_bf.shape, jnp.float32),
            jax.ShapeDtypeStruct(panel_t.shape, jnp.float32),
        ],
        compiler_params=pltpu.CompilerParams(dimension_semantics=("arbitrary",)),
        cost_estimate=pl.CostEstimate(flops=flops, bytes_accessed=moved_bytes, transcendentals=0),
    )(slot_of, live, user_bf, user_t, panel_bf, panel_t, *([blocks] * (TILES_PER_STEP * item_tiles)))


def local(user_factors, item_factors, stratum_masks, block_codes, block_counts, ratings):
    stratum_total = stratum_masks.shape[0]
    slot_count = block_codes.shape[-1] // stratum_total
    tile_size = ratings.shape[-1]
    all_blocks = ratings.reshape(-1, tile_size, tile_size)

    user_rows = user_factors
    panel_now = moved(item_factors, stratum_masks[0])
    for stratum in range(stratum_total):
        codes = block_codes[0, 0, stratum * slot_count : (stratum + 1) * slot_count]
        count = block_counts[0, 0, stratum]
        user_bf = user_rows.astype(jnp.bfloat16)
        panel_bf = panel_now.astype(jnp.bfloat16)
        grad_user, grad_panel_t = local_grads(
            user_bf, user_bf.T, panel_bf, panel_bf.T, codes, count, all_blocks, stratum * slot_count
        )
        panel_next = panel_now - LEARNING_RATE * (grad_panel_t.T + WEIGHT_DECAY * panel_now)
        if stratum + 1 < stratum_total:
            step_mask = jnp.bitwise_xor(stratum_masks[stratum], stratum_masks[stratum + 1])
        else:
            step_mask = stratum_masks[stratum]
        panel_now = moved(panel_next, step_mask)
        grad_total = item_sum(grad_user)
        user_rows = user_rows - LEARNING_RATE * (grad_total + WEIGHT_DECAY * user_rows)
    return (user_rows, panel_now)


def solution(mesh):
    placed = (
        P(("groups", "user"), None),
        P(("groups", "user", "item"), None),
        P("groups"),
        P(("groups", "user"), "item", None),
        P(("groups", "user"), "item", None),
        P(("groups", "user"), "item", None, None, None),
    )
    return jax.shard_map(
        local,
        mesh=mesh,
        in_specs=placed,
        out_specs=(P(("groups", "user"), None), P(("groups", "user", "item"), None)),
        check_vma=False,
    )
```

```python
import functools

import jax
import jax.numpy as jnp
from jax import lax
from jax.experimental import pallas as pl
from jax.experimental.pallas import tpu as pltpu
from jax.sharding import PartitionSpec as P

LEARNING_RATE = 0.02
WEIGHT_DECAY = 0.1
TILES_PER_STEP = 4


def moved(value, partner_mask):
    count = lax.axis_size("user")

    def branch(mask):
        if mask == 0:
            return lambda held: held
        pairs = [(source, source ^ mask) for source in range(count)]
        return lambda held: lax.ppermute(held, "user", pairs)

    return lax.switch(partner_mask, [branch(mask) for mask in range(count)], value)


def item_sum(value):
    if lax.axis_size("item") == 2:
        return value + lax.ppermute(value, "item", [(0, 1), (1, 0)])
    return lax.psum(value, "item")


def grads_kernel(item_tiles, slot_ref, live_ref, user_ref, panel_ref, *rest):
    block_refs = rest[: TILES_PER_STEP * item_tiles]
    grad_user_ref, grad_panel_ref = rest[TILES_PER_STEP * item_tiles :]
    step = pl.program_id(0)
    tile_size = block_refs[0].shape[-1]

    @pl.when(step == 0)
    def _():
        grad_panel_ref[...] = jnp.zeros_like(grad_panel_ref)

    user_bf = user_ref[...].astype(jnp.bfloat16)
    panel_bf = panel_ref[...]
    scores = lax.dot_general(
        user_bf, panel_bf, (((1,), (1,)), ((), ())), preferred_element_type=jnp.float32
    )
    pieces = []
    for inner in range(TILES_PER_STEP):
        row = []
        for column in range(item_tiles):
            code = (step * TILES_PER_STEP + inner) * item_tiles + column
            live = live_ref[code].astype(jnp.float32)
            block = block_refs[inner * item_tiles + column][...].astype(jnp.float32)
            part = scores[inner * tile_size : (inner + 1) * tile_size, column * tile_size : (column + 1) * tile_size]
            row.append(((part - block) * live).astype(jnp.bfloat16))
        pieces.append(jnp.concatenate(row, axis=1))
    errors = jnp.concatenate(pieces, axis=0)
    grad_user_ref[...] = jnp.dot(errors, panel_bf, preferred_element_type=jnp.float32)
    grad_panel_ref[...] += lax.dot_general(
        errors, user_bf, (((0,), (0,)), ((), ())), preferred_element_type=jnp.float32
    )


def local_grads(user_rows, panel_bf, codes, count, blocks, first):
    tile_size = blocks.shape[-1]
    rank = user_rows.shape[1]
    user_tiles = user_rows.shape[0] // tile_size
    item_tiles = panel_bf.shape[0] // tile_size
    code_count = user_tiles * item_tiles
    slot_count = codes.shape[0]
    hits = (codes[:, None] == lax.iota(jnp.int32, code_count)[None, :]) & (
        lax.iota(jnp.int32, slot_count) < count
    )[:, None]
    live = jnp.any(hits, axis=0).astype(jnp.int32)
    slot_of = first + jnp.sum(jnp.where(hits, lax.iota(jnp.int32, slot_count)[:, None], 0), axis=0)

    def block_spec(inner, column):
        def index(step, slot_ref, live_ref):
            return (slot_ref[(step * TILES_PER_STEP + inner) * item_tiles + column], 0, 0)

        return pl.BlockSpec((None, tile_size, tile_size), index)

    rows = TILES_PER_STEP * tile_size
    columns = item_tiles * tile_size
    grid_spec = pltpu.PrefetchScalarGridSpec(
        num_scalar_prefetch=2,
        grid=(user_tiles // TILES_PER_STEP,),
        in_specs=[
            pl.BlockSpec((rows, rank), lambda step, slot_ref, live_ref: (step, 0)),
            pl.BlockSpec((columns, rank), lambda step, slot_ref, live_ref: (0, 0)),
        ]
        + [block_spec(inner, column) for inner in range(TILES_PER_STEP) for column in range(item_tiles)],
        out_specs=[
            pl.BlockSpec((rows, rank), lambda step, slot_ref, live_ref: (step, 0)),
            pl.BlockSpec((columns, rank), lambda step, slot_ref, live_ref: (0, 0)),
        ],
    )
    flops = 3 * 2 * code_count * tile_size * tile_size * rank
    moved_bytes = user_rows.size * 8 + panel_bf.size * 6 + code_count * tile_size * tile_size * 2
    return pl.pallas_call(
        functools.partial(grads_kernel, item_tiles),
        grid_spec=grid_spec,
        out_shape=[
            jax.ShapeDtypeStruct(user_rows.shape, jnp.float32),
            jax.ShapeDtypeStruct(panel_bf.shape, jnp.float32),
        ],
        compiler_params=pltpu.CompilerParams(dimension_semantics=("arbitrary",)),
        cost_estimate=pl.CostEstimate(flops=flops, bytes_accessed=moved_bytes, transcendentals=0),
    )(slot_of, live, user_rows, panel_bf, *([blocks] * (TILES_PER_STEP * item_tiles)))


def local(user_factors, item_factors, stratum_masks, block_codes, block_counts, ratings):
    stratum_total = stratum_masks.shape[0]
    slot_count = block_codes.shape[-1] // stratum_total
    tile_size = ratings.shape[-1]
    all_blocks = ratings.reshape(-1, tile_size, tile_size)

    user_rows = user_factors
    panel_now = moved(item_factors, stratum_masks[0])
    for stratum in range(stratum_total):
        codes = block_codes[0, 0, stratum * slot_count : (stratum + 1) * slot_count]
        count = block_counts[0, 0, stratum]
        grad_user, grad_panel = local_grads(
            user_rows, panel_now.astype(jnp.bfloat16), codes, count, all_blocks, stratum * slot_count
        )
        panel_next = panel_now - LEARNING_RATE * (grad_panel + WEIGHT_DECAY * panel_now)
        if stratum + 1 < stratum_total:
            step_mask = jnp.bitwise_xor(stratum_masks[stratum], stratum_masks[stratum + 1])
        else:
            step_mask = stratum_masks[stratum]
        panel_now = moved(panel_next, step_mask)
        grad_total = item_sum(grad_user)
        user_rows = user_rows - LEARNING_RATE * (grad_total + WEIGHT_DECAY * user_rows)
    return (user_rows, panel_now)


def solution(mesh):
    placed = (
        P(("groups", "user"), None),
        P(("groups", "user", "item"), None),
        P("groups"),
        P(("groups", "user"), "item", None),
        P(("groups", "user"), "item", None),
        P(("groups", "user"), "item", None, None, None),
    )
    return jax.shard_map(
        local,
        mesh=mesh,
        in_specs=placed,
        out_specs=(P(("groups", "user"), None), P(("groups", "user", "item"), None)),
        check_vma=False,
    )
```

```python
import functools

import jax
import jax.numpy as jnp
from jax import lax
from jax.experimental import pallas as pl
from jax.experimental.pallas import tpu as pltpu
from jax.sharding import PartitionSpec as P

LEARNING_RATE = 0.02
WEIGHT_DECAY = 0.1
TILES_PER_STEP = 4


def moved(value, partner_mask, work):
    count = lax.axis_size("user")

    def branch(mask):
        def run(held):
            done = work()
            if mask == 0:
                return held, done
            pairs = [(source, source ^ mask) for source in range(count)]
            return lax.ppermute(held, "user", pairs), done

        return run

    return lax.switch(partner_mask, [branch(mask) for mask in range(count)], value)


def item_sum(value):
    if lax.axis_size("item") == 2:
        return value + lax.ppermute(value, "item", [(0, 1), (1, 0)])
    return lax.psum(value, "item")


def grads_kernel(item_tiles, slot_ref, live_ref, user_ref, panel_ref, *rest):
    block_refs = rest[: TILES_PER_STEP * item_tiles]
    grad_user_ref, grad_panel_ref = rest[TILES_PER_STEP * item_tiles :]
    step = pl.program_id(0)
    tile_size = block_refs[0].shape[-1]

    @pl.when(step == 0)
    def _():
        grad_panel_ref[...] = jnp.zeros_like(grad_panel_ref)

    user_bf = user_ref[...].astype(jnp.bfloat16)
    panel_bf = panel_ref[...]
    scores = lax.dot_general(
        user_bf, panel_bf, (((1,), (1,)), ((), ())), preferred_element_type=jnp.float32
    )
    pieces = []
    for inner in range(TILES_PER_STEP):
        row = []
        for column in range(item_tiles):
            code = (step * TILES_PER_STEP + inner) * item_tiles + column
            live = live_ref[code].astype(jnp.float32)
            block = block_refs[inner * item_tiles + column][...].astype(jnp.float32)
            part = scores[inner * tile_size : (inner + 1) * tile_size, column * tile_size : (column + 1) * tile_size]
            row.append(((part - block) * live).astype(jnp.bfloat16))
        pieces.append(jnp.concatenate(row, axis=1))
    errors = jnp.concatenate(pieces, axis=0)
    grad_user_ref[...] = jnp.dot(errors, panel_bf, preferred_element_type=jnp.float32)
    grad_panel_ref[...] += lax.dot_general(
        errors, user_bf, (((0,), (0,)), ((), ())), preferred_element_type=jnp.float32
    )


def slot_tables(codes, count, first, code_count):
    slot_count = codes.shape[0]
    hits = (codes[:, None] == lax.iota(jnp.int32, code_count)[None, :]) & (
        lax.iota(jnp.int32, slot_count) < count
    )[:, None]
    live = jnp.any(hits, axis=0).astype(jnp.int32)
    slot_of = first + jnp.sum(jnp.where(hits, lax.iota(jnp.int32, slot_count)[:, None], 0), axis=0)
    return slot_of, live


def local_grads(user_rows, panel_bf, tables, blocks):
    slot_of, live = tables
    tile_size = blocks.shape[-1]
    rank = user_rows.shape[1]
    user_tiles = user_rows.shape[0] // tile_size
    item_tiles = panel_bf.shape[0] // tile_size
    code_count = user_tiles * item_tiles

    def block_spec(inner, column):
        def index(step, slot_ref, live_ref):
            return (slot_ref[(step * TILES_PER_STEP + inner) * item_tiles + column], 0, 0)

        return pl.BlockSpec((None, tile_size, tile_size), index)

    rows = TILES_PER_STEP * tile_size
    columns = item_tiles * tile_size
    grid_spec = pltpu.PrefetchScalarGridSpec(
        num_scalar_prefetch=2,
        grid=(user_tiles // TILES_PER_STEP,),
        in_specs=[
            pl.BlockSpec((rows, rank), lambda step, slot_ref, live_ref: (step, 0)),
            pl.BlockSpec((columns, rank), lambda step, slot_ref, live_ref: (0, 0)),
        ]
        + [block_spec(inner, column) for inner in range(TILES_PER_STEP) for column in range(item_tiles)],
        out_specs=[
            pl.BlockSpec((rows, rank), lambda step, slot_ref, live_ref: (step, 0)),
            pl.BlockSpec((columns, rank), lambda step, slot_ref, live_ref: (0, 0)),
        ],
    )
    flops = 3 * 2 * code_count * tile_size * tile_size * rank
    moved_bytes = user_rows.size * 8 + panel_bf.size * 6 + code_count * tile_size * tile_size * 2
    return pl.pallas_call(
        functools.partial(grads_kernel, item_tiles),
        grid_spec=grid_spec,
        out_shape=[
            jax.ShapeDtypeStruct(user_rows.shape, jnp.float32),
            jax.ShapeDtypeStruct(panel_bf.shape, jnp.float32),
        ],
        compiler_params=pltpu.CompilerParams(dimension_semantics=("arbitrary",)),
        cost_estimate=pl.CostEstimate(flops=flops, bytes_accessed=moved_bytes, transcendentals=0),
    )(slot_of, live, user_rows, panel_bf, *([blocks] * (TILES_PER_STEP * item_tiles)))


def local(user_factors, item_factors, stratum_masks, block_codes, block_counts, ratings):
    stratum_total = stratum_masks.shape[0]
    slot_count = block_codes.shape[-1] // stratum_total
    tile_size = ratings.shape[-1]
    code_count = (user_factors.shape[0] // tile_size) * (item_factors.shape[0] // tile_size)
    all_blocks = ratings.reshape(-1, tile_size, tile_size)

    def tables(stratum):
        codes = block_codes[0, 0, stratum * slot_count : (stratum + 1) * slot_count]
        count = block_counts[0, 0, stratum]
        return slot_tables(codes, count, stratum * slot_count, code_count)

    user_rows = user_factors
    panel_now, ready = moved(item_factors, stratum_masks[0], lambda: tables(0))
    for stratum in range(stratum_total):
        grad_user, grad_panel = local_grads(user_rows, panel_now.astype(jnp.bfloat16), ready, all_blocks)
        panel_next = panel_now - LEARNING_RATE * (grad_panel + WEIGHT_DECAY * panel_now)
        last = stratum + 1 == stratum_total
        if last:
            step_mask = stratum_masks[stratum]
        else:
            step_mask = jnp.bitwise_xor(stratum_masks[stratum], stratum_masks[stratum + 1])

        def user_step(grad_user=grad_user, user_rows=user_rows, last=last, stratum=stratum):
            grad_total = item_sum(grad_user)
            rows = user_rows - LEARNING_RATE * (grad_total + WEIGHT_DECAY * user_rows)
            return rows, (None if last else tables(stratum + 1))

        panel_now, (user_rows, ready) = moved(panel_next, step_mask, user_step)
    return (user_rows, panel_now)


def solution(mesh):
    placed = (
        P(("groups", "user"), None),
        P(("groups", "user", "item"), None),
        P("groups"),
        P(("groups", "user"), "item", None),
        P(("groups", "user"), "item", None),
        P(("groups", "user"), "item", None, None, None),
    )
    return jax.shard_map(
        local,
        mesh=mesh,
        in_specs=placed,
        out_specs=(P(("groups", "user"), None), P(("groups", "user", "item"), None)),
        check_vma=False,
    )
```

```python
import functools

import jax
import jax.numpy as jnp
from jax import lax
from jax.experimental import pallas as pl
from jax.experimental.pallas import tpu as pltpu
from jax.sharding import PartitionSpec as P

LEARNING_RATE = 0.02
WEIGHT_DECAY = 0.1
TILES_PER_STEP = 4


def moved(value, partner_mask, work):
    count = lax.axis_size("user")

    def branch(mask):
        def run(held):
            done = work()
            if mask == 0:
                return held, done
            pairs = [(source, source ^ mask) for source in range(count)]
            return lax.ppermute(held, "user", pairs), done

        return run

    return lax.switch(partner_mask, [branch(mask) for mask in range(count)], value)


def item_sum(value):
    if lax.axis_size("item") == 2:
        return value + lax.ppermute(value, "item", [(0, 1), (1, 0)])
    return lax.psum(value, "item")


def grads_kernel(item_tiles, code_stride, offset, summed, slot_ref, live_ref, user_ref, panel_ref, *rest):
    block_refs = rest[: TILES_PER_STEP * item_tiles]
    rest = rest[TILES_PER_STEP * item_tiles :]
    earlier_ref = rest[0] if summed else None
    grad_user_ref, grad_panel_ref = rest[1:] if summed else rest
    step = pl.program_id(0)
    tile_size = block_refs[0].shape[-1]

    @pl.when(step == 0)
    def _():
        grad_panel_ref[...] = jnp.zeros_like(grad_panel_ref)

    user_bf = user_ref[...].astype(jnp.bfloat16)
    panel_bf = panel_ref[...]
    scores = lax.dot_general(
        user_bf, panel_bf, (((1,), (1,)), ((), ())), preferred_element_type=jnp.float32
    )
    pieces = []
    for inner in range(TILES_PER_STEP):
        row = []
        for column in range(item_tiles):
            code = (step * TILES_PER_STEP + inner) * code_stride + offset + column
            live = live_ref[code].astype(jnp.float32)
            block = block_refs[inner * item_tiles + column][...].astype(jnp.float32)
            part = scores[inner * tile_size : (inner + 1) * tile_size, column * tile_size : (column + 1) * tile_size]
            row.append(((part - block) * live).astype(jnp.bfloat16))
        pieces.append(jnp.concatenate(row, axis=1))
    errors = jnp.concatenate(pieces, axis=0)
    grad_user = jnp.dot(errors, panel_bf, preferred_element_type=jnp.float32)
    grad_user_ref[...] = grad_user + earlier_ref[...] if summed else grad_user
    grad_panel_ref[...] += lax.dot_general(
        errors, user_bf, (((0,), (0,)), ((), ())), preferred_element_type=jnp.float32
    )


def slot_tables(codes, count, first, code_count):
    slot_count = codes.shape[0]
    hits = (codes[:, None] == lax.iota(jnp.int32, code_count)[None, :]) & (
        lax.iota(jnp.int32, slot_count) < count
    )[:, None]
    live = jnp.any(hits, axis=0).astype(jnp.int32)
    slot_of = first + jnp.sum(jnp.where(hits, lax.iota(jnp.int32, slot_count)[:, None], 0), axis=0)
    return slot_of, live


def local_grads(user_rows, panel_bf, tables, blocks, code_stride, offset, earlier=None):
    slot_of, live = tables
    tile_size = blocks.shape[-1]
    rank = user_rows.shape[1]
    user_tiles = user_rows.shape[0] // tile_size
    item_tiles = panel_bf.shape[0] // tile_size
    code_count = user_tiles * item_tiles
    summed = earlier is not None

    def block_spec(inner, column):
        def index(step, slot_ref, live_ref):
            return (slot_ref[(step * TILES_PER_STEP + inner) * code_stride + offset + column], 0, 0)

        return pl.BlockSpec((None, tile_size, tile_size), index)

    rows = TILES_PER_STEP * tile_size
    columns = item_tiles * tile_size
    user_spec = pl.BlockSpec((rows, rank), lambda step, slot_ref, live_ref: (step, 0))
    grid_spec = pltpu.PrefetchScalarGridSpec(
        num_scalar_prefetch=2,
        grid=(user_tiles // TILES_PER_STEP,),
        in_specs=[user_spec, pl.BlockSpec((columns, rank), lambda step, slot_ref, live_ref: (0, 0))]
        + [block_spec(inner, column) for inner in range(TILES_PER_STEP) for column in range(item_tiles)]
        + ([user_spec] if summed else []),
        out_specs=[user_spec, pl.BlockSpec((columns, rank), lambda step, slot_ref, live_ref: (0, 0))],
    )
    flops = 3 * 2 * code_count * tile_size * tile_size * rank
    moved_bytes = user_rows.size * (12 if summed else 8) + panel_bf.size * 6 + code_count * tile_size * tile_size * 2
    operands = [slot_of, live, user_rows, panel_bf] + [blocks] * (TILES_PER_STEP * item_tiles)
    return pl.pallas_call(
        functools.partial(grads_kernel, item_tiles, code_stride, offset, summed),
        grid_spec=grid_spec,
        out_shape=[
            jax.ShapeDtypeStruct(user_rows.shape, jnp.float32),
            jax.ShapeDtypeStruct(panel_bf.shape, jnp.float32),
        ],
        input_output_aliases={len(operands): 0} if summed else {},
        compiler_params=pltpu.CompilerParams(dimension_semantics=("arbitrary",)),
        cost_estimate=pl.CostEstimate(flops=flops, bytes_accessed=moved_bytes, transcendentals=0),
    )(*operands, *([earlier] if summed else []))


def local(user_factors, item_factors, stratum_masks, block_codes, block_counts, ratings):
    stratum_total = stratum_masks.shape[0]
    slot_count = block_codes.shape[-1] // stratum_total
    tile_size = ratings.shape[-1]
    item_tiles = item_factors.shape[0] // tile_size
    code_count = (user_factors.shape[0] // tile_size) * item_tiles
    all_blocks = ratings.reshape(-1, tile_size, tile_size)
    half_tiles = item_tiles // 2
    half_rows = half_tiles * tile_size

    def tables(stratum):
        codes = block_codes[0, 0, stratum * slot_count : (stratum + 1) * slot_count]
        count = block_counts[0, 0, stratum]
        return slot_tables(codes, count, stratum * slot_count, code_count)

    def half_step(user_rows, panel_half, ready, half, earlier):
        grad_user, grad_panel = local_grads(
            user_rows, panel_half.astype(jnp.bfloat16), ready, all_blocks, item_tiles, half * half_tiles, earlier
        )
        return grad_user, panel_half - LEARNING_RATE * (grad_panel + WEIGHT_DECAY * panel_half)

    def step_mask(stratum):
        if stratum + 1 == stratum_total:
            return stratum_masks[stratum]
        return jnp.bitwise_xor(stratum_masks[stratum], stratum_masks[stratum + 1])

    first_half, ready = moved(item_factors[:half_rows], stratum_masks[0], lambda: tables(0))
    user_rows = user_factors
    grad_user = None
    done_first = None
    second_in = item_factors[half_rows:]
    second_mask = stratum_masks[0]
    for stratum in range(stratum_total):
        last = stratum + 1 == stratum_total
        if done_first is None:
            second_half, (grad_user, done_first) = moved(
                second_in, second_mask,
                lambda: half_step(user_rows, first_half, ready, 0, None),
            )
        out_first, (grad_user, done_second) = moved(
            done_first, step_mask(stratum),
            lambda: half_step(user_rows, second_half, ready, 1, grad_user),
        )

        def user_step(grad_user=grad_user, user_rows=user_rows, last=last, stratum=stratum, out_first=out_first):
            grad_total = item_sum(grad_user)
            rows = user_rows - LEARNING_RATE * (grad_total + WEIGHT_DECAY * user_rows)
            if last:
                return rows, None, None, None
            ready_next = tables(stratum + 1)
            grad_next, first_next = half_step(rows, out_first, ready_next, 0, None)
            return rows, ready_next, grad_next, first_next

        out_second, (user_rows, ready, grad_user, done_first) = moved(done_second, step_mask(stratum), user_step)
        first_half, second_half = out_first, out_second
    return (user_rows, jnp.concatenate([first_half, second_half], axis=0))


def solution(mesh):
    placed = (
        P(("groups", "user"), None),
        P(("groups", "user", "item"), None),
        P("groups"),
        P(("groups", "user"), "item", None),
        P(("groups", "user"), "item", None),
        P(("groups", "user"), "item", None, None, None),
    )
    return jax.shard_map(
        local,
        mesh=mesh,
        in_specs=placed,
        out_specs=(P(("groups", "user"), None), P(("groups", "user", "item"), None)),
        check_vma=False,
    )
```

```python
import functools

import jax
import jax.numpy as jnp
from jax import lax
from jax.experimental import pallas as pl
from jax.experimental.pallas import tpu as pltpu
from jax.sharding import PartitionSpec as P

LEARNING_RATE = 0.02
WEIGHT_DECAY = 0.1
TILES_PER_STEP = 8


def moved(value, partner_mask, work):
    count = lax.axis_size("user")

    def branch(mask):
        def run(held):
            done = work()
            if mask == 0:
                return held, done
            pairs = [(source, source ^ mask) for source in range(count)]
            return lax.optimization_barrier((lax.ppermute(held, "user", pairs), done))

        return run

    return lax.switch(partner_mask, [branch(mask) for mask in range(count)], value)


def item_sum(value):
    if lax.axis_size("item") == 2:
        return value + lax.ppermute(value, "item", [(0, 1), (1, 0)])
    return lax.psum(value, "item")


def grads_kernel(item_tiles, slot_ref, live_ref, user_ref, panel_ref, *rest):
    block_refs = rest[: TILES_PER_STEP * item_tiles]
    grad_user_ref, grad_panel_ref = rest[TILES_PER_STEP * item_tiles :]
    step = pl.program_id(0)
    tile_size = block_refs[0].shape[-1]

    @pl.when(step == 0)
    def _():
        grad_panel_ref[...] = jnp.zeros_like(grad_panel_ref)

    user_bf = user_ref[...].astype(jnp.bfloat16)
    panel_bf = panel_ref[...]
    scores = lax.dot_general(
        user_bf, panel_bf, (((1,), (1,)), ((), ())), preferred_element_type=jnp.float32
    )
    pieces = []
    for inner in range(TILES_PER_STEP):
        row = []
        for column in range(item_tiles):
            code = (step * TILES_PER_STEP + inner) * item_tiles + column
            live = live_ref[code].astype(jnp.float32)
            block = block_refs[inner * item_tiles + column][...].astype(jnp.float32)
            part = scores[inner * tile_size : (inner + 1) * tile_size, column * tile_size : (column + 1) * tile_size]
            row.append(((part - block) * live).astype(jnp.bfloat16))
        pieces.append(jnp.concatenate(row, axis=1))
    errors = jnp.concatenate(pieces, axis=0)
    grad_user_ref[...] = jnp.dot(errors, panel_bf, preferred_element_type=jnp.float32)
    grad_panel_ref[...] += lax.dot_general(
        errors, user_bf, (((0,), (0,)), ((), ())), preferred_element_type=jnp.float32
    )


def slot_tables(codes, count, first, code_count):
    slot_count = codes.shape[0]
    hits = (codes[:, None] == lax.iota(jnp.int32, code_count)[None, :]) & (
        lax.iota(jnp.int32, slot_count) < count
    )[:, None]
    live = jnp.any(hits, axis=0).astype(jnp.int32)
    slot_of = first + jnp.sum(jnp.where(hits, lax.iota(jnp.int32, slot_count)[:, None], 0), axis=0)
    return slot_of, live


def local_grads(user_rows, panel_bf, tables, blocks):
    slot_of, live = tables
    tile_size = blocks.shape[-1]
    rank = user_rows.shape[1]
    user_tiles = user_rows.shape[0] // tile_size
    item_tiles = panel_bf.shape[0] // tile_size
    code_count = user_tiles * item_tiles

    def block_spec(inner, column):
        def index(step, slot_ref, live_ref):
            return (slot_ref[(step * TILES_PER_STEP + inner) * item_tiles + column], 0, 0)

        return pl.BlockSpec((None, tile_size, tile_size), index)

    rows = TILES_PER_STEP * tile_size
    columns = item_tiles * tile_size
    grid_spec = pltpu.PrefetchScalarGridSpec(
        num_scalar_prefetch=2,
        grid=(user_tiles // TILES_PER_STEP,),
        in_specs=[
            pl.BlockSpec((rows, rank), lambda step, slot_ref, live_ref: (step, 0)),
            pl.BlockSpec((columns, rank), lambda step, slot_ref, live_ref: (0, 0)),
        ]
        + [block_spec(inner, column) for inner in range(TILES_PER_STEP) for column in range(item_tiles)],
        out_specs=[
            pl.BlockSpec((rows, rank), lambda step, slot_ref, live_ref: (step, 0)),
            pl.BlockSpec((columns, rank), lambda step, slot_ref, live_ref: (0, 0)),
        ],
    )
    flops = 3 * 2 * code_count * tile_size * tile_size * rank
    moved_bytes = user_rows.size * 8 + panel_bf.size * 6 + code_count * tile_size * tile_size * 2
    return pl.pallas_call(
        functools.partial(grads_kernel, item_tiles),
        grid_spec=grid_spec,
        out_shape=[
            jax.ShapeDtypeStruct(user_rows.shape, jnp.float32),
            jax.ShapeDtypeStruct(panel_bf.shape, jnp.float32),
        ],
        compiler_params=pltpu.CompilerParams(dimension_semantics=("arbitrary",)),
        cost_estimate=pl.CostEstimate(flops=flops, bytes_accessed=moved_bytes, transcendentals=0),
    )(slot_of, live, user_rows, panel_bf, *([blocks] * (TILES_PER_STEP * item_tiles)))


def local(user_factors, item_factors, stratum_masks, block_codes, block_counts, ratings):
    stratum_total = stratum_masks.shape[0]
    slot_count = block_codes.shape[-1] // stratum_total
    tile_size = ratings.shape[-1]
    code_count = (user_factors.shape[0] // tile_size) * (item_factors.shape[0] // tile_size)
    all_blocks = ratings.reshape(-1, tile_size, tile_size)

    def tables(stratum):
        codes = block_codes[0, 0, stratum * slot_count : (stratum + 1) * slot_count]
        count = block_counts[0, 0, stratum]
        return slot_tables(codes, count, stratum * slot_count, code_count)

    user_rows = user_factors
    panel_now, ready = moved(item_factors, stratum_masks[0], lambda: tables(0))
    for stratum in range(stratum_total):
        grad_user, grad_panel = local_grads(user_rows, panel_now.astype(jnp.bfloat16), ready, all_blocks)
        panel_next = panel_now - LEARNING_RATE * (grad_panel + WEIGHT_DECAY * panel_now)
        last = stratum + 1 == stratum_total
        if last:
            step_mask = stratum_masks[stratum]
        else:
            step_mask = jnp.bitwise_xor(stratum_masks[stratum], stratum_masks[stratum + 1])

        def user_step(grad_user=grad_user, user_rows=user_rows, last=last, stratum=stratum):
            grad_total = item_sum(grad_user)
            rows = user_rows - LEARNING_RATE * (grad_total + WEIGHT_DECAY * user_rows)
            return rows, (None if last else tables(stratum + 1))

        panel_now, (user_rows, ready) = moved(panel_next, step_mask, user_step)
    return (user_rows, panel_now)


def solution(mesh):
    placed = (
        P(("groups", "user"), None),
        P(("groups", "user", "item"), None),
        P("groups"),
        P(("groups", "user"), "item", None),
        P(("groups", "user"), "item", None),
        P(("groups", "user"), "item", None, None, None),
    )
    return jax.shard_map(
        local,
        mesh=mesh,
        in_specs=placed,
        out_specs=(P(("groups", "user"), None), P(("groups", "user", "item"), None)),
        check_vma=False,
    )
```

```python
import functools

import jax
import jax.numpy as jnp
from jax import lax
from jax.experimental import pallas as pl
from jax.experimental.pallas import tpu as pltpu
from jax.sharding import PartitionSpec as P

LEARNING_RATE = 0.02
WEIGHT_DECAY = 0.1
TILES_PER_STEP = 8


def moved(value, partner_mask, work, may_stay):
    count = lax.axis_size("user")

    def branch(mask):
        def run(held):
            done = work()
            if mask == 0:
                return held, done
            pairs = [(source, source ^ mask) for source in range(count)]
            return lax.optimization_barrier((lax.ppermute(held, "user", pairs), done))

        return run

    if may_stay:
        return lax.switch(partner_mask, [branch(mask) for mask in range(count)], value)
    return lax.switch(partner_mask - 1, [branch(mask) for mask in range(1, count)], value)


def item_sum(value):
    if lax.axis_size("item") == 2:
        return value + lax.ppermute(value, "item", [(0, 1), (1, 0)])
    return lax.psum(value, "item")


def grads_kernel(item_tiles, slot_ref, live_ref, user_ref, panel_ref, *rest):
    block_refs = rest[: TILES_PER_STEP * item_tiles]
    grad_user_ref, grad_panel_ref, panel_bf_ref = rest[TILES_PER_STEP * item_tiles :]
    step = pl.program_id(0)
    tile_size = block_refs[0].shape[-1]

    @pl.when(step == 0)
    def _():
        grad_panel_ref[...] = jnp.zeros_like(grad_panel_ref)
        panel_bf_ref[...] = panel_ref[...].astype(jnp.bfloat16)

    user_bf = user_ref[...].astype(jnp.bfloat16)
    panel_bf = panel_bf_ref[...]
    scores = lax.dot_general(
        user_bf, panel_bf, (((1,), (1,)), ((), ())), preferred_element_type=jnp.float32
    )
    pieces = []
    for inner in range(TILES_PER_STEP):
        row = []
        for column in range(item_tiles):
            code = (step * TILES_PER_STEP + inner) * item_tiles + column
            live = live_ref[code].astype(jnp.float32)
            block = block_refs[inner * item_tiles + column][...].astype(jnp.float32)
            part = scores[inner * tile_size : (inner + 1) * tile_size, column * tile_size : (column + 1) * tile_size]
            row.append(((part - block) * live).astype(jnp.bfloat16))
        pieces.append(jnp.concatenate(row, axis=1))
    errors = jnp.concatenate(pieces, axis=0)
    grad_user_ref[...] = jnp.dot(errors, panel_bf, preferred_element_type=jnp.float32)
    grad_panel_ref[...] += lax.dot_general(
        errors, user_bf, (((0,), (0,)), ((), ())), preferred_element_type=jnp.float32
    )


def slot_tables(codes, count, first, code_count):
    slot_count = codes.shape[0]
    hits = (codes[:, None] == lax.iota(jnp.int32, code_count)[None, :]) & (
        lax.iota(jnp.int32, slot_count) < count
    )[:, None]
    live = jnp.any(hits, axis=0).astype(jnp.int32)
    slot_of = first + jnp.sum(jnp.where(hits, lax.iota(jnp.int32, slot_count)[:, None], 0), axis=0)
    return slot_of, live


def local_grads(user_rows, panel_bf, tables, blocks):
    slot_of, live = tables
    tile_size = blocks.shape[-1]
    rank = user_rows.shape[1]
    user_tiles = user_rows.shape[0] // tile_size
    item_tiles = panel_bf.shape[0] // tile_size
    code_count = user_tiles * item_tiles

    def block_spec(inner, column):
        def index(step, slot_ref, live_ref):
            return (slot_ref[(step * TILES_PER_STEP + inner) * item_tiles + column], 0, 0)

        return pl.BlockSpec((None, tile_size, tile_size), index)

    rows = TILES_PER_STEP * tile_size
    columns = item_tiles * tile_size
    grid_spec = pltpu.PrefetchScalarGridSpec(
        num_scalar_prefetch=2,
        grid=(user_tiles // TILES_PER_STEP,),
        in_specs=[
            pl.BlockSpec((rows, rank), lambda step, slot_ref, live_ref: (step, 0)),
            pl.BlockSpec((columns, rank), lambda step, slot_ref, live_ref: (0, 0)),
        ]
        + [block_spec(inner, column) for inner in range(TILES_PER_STEP) for column in range(item_tiles)],
        out_specs=[
            pl.BlockSpec((rows, rank), lambda step, slot_ref, live_ref: (step, 0)),
            pl.BlockSpec((columns, rank), lambda step, slot_ref, live_ref: (0, 0)),
        ],
        scratch_shapes=[pltpu.VMEM((columns, rank), jnp.bfloat16)],
    )
    flops = 3 * 2 * code_count * tile_size * tile_size * rank
    moved_bytes = user_rows.size * 8 + panel_bf.size * 8 + code_count * tile_size * tile_size * 2
    return pl.pallas_call(
        functools.partial(grads_kernel, item_tiles),
        grid_spec=grid_spec,
        out_shape=[
            jax.ShapeDtypeStruct(user_rows.shape, jnp.float32),
            jax.ShapeDtypeStruct(panel_bf.shape, jnp.float32),
        ],
        compiler_params=pltpu.CompilerParams(dimension_semantics=("arbitrary",)),
        cost_estimate=pl.CostEstimate(flops=flops, bytes_accessed=moved_bytes, transcendentals=0),
    )(slot_of, live, user_rows, panel_bf, *([blocks] * (TILES_PER_STEP * item_tiles)))


def local(user_factors, item_factors, stratum_masks, block_codes, block_counts, ratings):
    stratum_total = stratum_masks.shape[0]
    slot_count = block_codes.shape[-1] // stratum_total
    tile_size = ratings.shape[-1]
    code_count = (user_factors.shape[0] // tile_size) * (item_factors.shape[0] // tile_size)
    all_blocks = ratings.reshape(-1, tile_size, tile_size)

    def tables(stratum):
        codes = block_codes[0, 0, stratum * slot_count : (stratum + 1) * slot_count]
        count = block_counts[0, 0, stratum]
        return slot_tables(codes, count, stratum * slot_count, code_count)

    user_rows = user_factors
    panel_now, ready = moved(item_factors, stratum_masks[0], lambda: tables(0), False)
    for stratum in range(stratum_total):
        grad_user, grad_panel = local_grads(user_rows, panel_now, ready, all_blocks)
        panel_next = panel_now - LEARNING_RATE * (grad_panel + WEIGHT_DECAY * panel_now)
        last = stratum + 1 == stratum_total
        if last:
            step_mask = stratum_masks[stratum]
        else:
            step_mask = jnp.bitwise_xor(stratum_masks[stratum], stratum_masks[stratum + 1])

        def user_step(grad_user=grad_user, user_rows=user_rows, last=last, stratum=stratum):
            grad_total = item_sum(grad_user)
            rows = user_rows - LEARNING_RATE * (grad_total + WEIGHT_DECAY * user_rows)
            return rows, (None if last else tables(stratum + 1))

        panel_now, (user_rows, ready) = moved(panel_next, step_mask, user_step, not last)
    return (user_rows, panel_now)


def solution(mesh):
    placed = (
        P(("groups", "user"), None),
        P(("groups", "user", "item"), None),
        P("groups"),
        P(("groups", "user"), "item", None),
        P(("groups", "user"), "item", None),
        P(("groups", "user"), "item", None, None, None),
    )
    return jax.shard_map(
        local,
        mesh=mesh,
        in_specs=placed,
        out_specs=(P(("groups", "user"), None), P(("groups", "user", "item"), None)),
        check_vma=False,
    )
```

```python
import functools

import jax
import jax.numpy as jnp
from jax import lax
from jax.experimental import pallas as pl
from jax.experimental.pallas import tpu as pltpu
from jax.sharding import PartitionSpec as P

LEARNING_RATE = 0.02
WEIGHT_DECAY = 0.1
TILES_PER_STEP = 8


def moved(value, partner_mask, work, may_stay):
    count = lax.axis_size("user")

    def branch(mask):
        def run(held):
            done = work()
            if mask == 0:
                return held, done
            pairs = [(source, source ^ mask) for source in range(count)]
            return lax.optimization_barrier((lax.ppermute(held, "user", pairs), done))

        return run

    if may_stay:
        return lax.switch(partner_mask, [branch(mask) for mask in range(count)], value)
    return lax.switch(partner_mask - 1, [branch(mask) for mask in range(1, count)], value)


def item_sum(value):
    if lax.axis_size("item") == 2:
        return value + lax.ppermute(value, "item", [(0, 1), (1, 0)])
    return lax.psum(value, "item")


def grads_kernel(item_tiles, slot_ref, live_ref, user_ref, panel_ref, *rest):
    block_refs = rest[: TILES_PER_STEP * item_tiles]
    grad_user_ref, panel_next_ref, panel_bf_ref, grad_panel_ref = rest[TILES_PER_STEP * item_tiles :]
    step = pl.program_id(0)
    tile_size = block_refs[0].shape[-1]

    @pl.when(step == 0)
    def _():
        grad_panel_ref[...] = jnp.zeros_like(grad_panel_ref)
        panel_bf_ref[...] = panel_ref[...].astype(jnp.bfloat16)

    user_bf = user_ref[...].astype(jnp.bfloat16)
    panel_bf = panel_bf_ref[...]
    scores = lax.dot_general(
        user_bf, panel_bf, (((1,), (1,)), ((), ())), preferred_element_type=jnp.float32
    )
    pieces = []
    for inner in range(TILES_PER_STEP):
        row = []
        for column in range(item_tiles):
            code = (step * TILES_PER_STEP + inner) * item_tiles + column
            live = live_ref[code].astype(jnp.float32)
            block = block_refs[inner * item_tiles + column][...].astype(jnp.float32)
            part = scores[inner * tile_size : (inner + 1) * tile_size, column * tile_size : (column + 1) * tile_size]
            row.append(((part - block) * live).astype(jnp.bfloat16))
        pieces.append(jnp.concatenate(row, axis=1))
    errors = jnp.concatenate(pieces, axis=0)
    grad_user_ref[...] = jnp.dot(errors, panel_bf, preferred_element_type=jnp.float32)
    grad_panel_ref[...] += lax.dot_general(
        errors, user_bf, (((0,), (0,)), ((), ())), preferred_element_type=jnp.float32
    )

    @pl.when(step == pl.num_programs(0) - 1)
    def _():
        panel = panel_ref[...]
        panel_next_ref[...] = panel - LEARNING_RATE * (grad_panel_ref[...] + WEIGHT_DECAY * panel)


def slot_tables(codes, count, first, code_count):
    slot_count = codes.shape[0]
    hits = (codes[:, None] == lax.iota(jnp.int32, code_count)[None, :]) & (
        lax.iota(jnp.int32, slot_count) < count
    )[:, None]
    live = jnp.any(hits, axis=0).astype(jnp.int32)
    slot_of = first + jnp.sum(jnp.where(hits, lax.iota(jnp.int32, slot_count)[:, None], 0), axis=0)
    return slot_of, live


def local_grads(user_rows, panel_bf, tables, blocks):
    slot_of, live = tables
    tile_size = blocks.shape[-1]
    rank = user_rows.shape[1]
    user_tiles = user_rows.shape[0] // tile_size
    item_tiles = panel_bf.shape[0] // tile_size
    code_count = user_tiles * item_tiles

    def block_spec(inner, column):
        def index(step, slot_ref, live_ref):
            return (slot_ref[(step * TILES_PER_STEP + inner) * item_tiles + column], 0, 0)

        return pl.BlockSpec((None, tile_size, tile_size), index)

    rows = TILES_PER_STEP * tile_size
    columns = item_tiles * tile_size
    grid_spec = pltpu.PrefetchScalarGridSpec(
        num_scalar_prefetch=2,
        grid=(user_tiles // TILES_PER_STEP,),
        in_specs=[
            pl.BlockSpec((rows, rank), lambda step, slot_ref, live_ref: (step, 0)),
            pl.BlockSpec((columns, rank), lambda step, slot_ref, live_ref: (0, 0)),
        ]
        + [block_spec(inner, column) for inner in range(TILES_PER_STEP) for column in range(item_tiles)],
        out_specs=[
            pl.BlockSpec((rows, rank), lambda step, slot_ref, live_ref: (step, 0)),
            pl.BlockSpec((columns, rank), lambda step, slot_ref, live_ref: (0, 0)),
        ],
        scratch_shapes=[pltpu.VMEM((columns, rank), jnp.bfloat16), pltpu.VMEM((columns, rank), jnp.float32)],
    )
    flops = 3 * 2 * code_count * tile_size * tile_size * rank
    moved_bytes = user_rows.size * 8 + panel_bf.size * 8 + code_count * tile_size * tile_size * 2
    return pl.pallas_call(
        functools.partial(grads_kernel, item_tiles),
        grid_spec=grid_spec,
        out_shape=[
            jax.ShapeDtypeStruct(user_rows.shape, jnp.float32),
            jax.ShapeDtypeStruct(panel_bf.shape, jnp.float32),
        ],
        compiler_params=pltpu.CompilerParams(dimension_semantics=("arbitrary",)),
        cost_estimate=pl.CostEstimate(flops=flops, bytes_accessed=moved_bytes, transcendentals=0),
    )(slot_of, live, user_rows, panel_bf, *([blocks] * (TILES_PER_STEP * item_tiles)))


def local(user_factors, item_factors, stratum_masks, block_codes, block_counts, ratings):
    stratum_total = stratum_masks.shape[0]
    slot_count = block_codes.shape[-1] // stratum_total
    tile_size = ratings.shape[-1]
    code_count = (user_factors.shape[0] // tile_size) * (item_factors.shape[0] // tile_size)
    all_blocks = ratings.reshape(-1, tile_size, tile_size)

    def tables(stratum):
        codes = block_codes[0, 0, stratum * slot_count : (stratum + 1) * slot_count]
        count = block_counts[0, 0, stratum]
        return slot_tables(codes, count, stratum * slot_count, code_count)

    user_rows = user_factors
    panel_now, ready = moved(item_factors, stratum_masks[0], lambda: tables(0), False)
    for stratum in range(stratum_total):
        grad_user, panel_next = local_grads(user_rows, panel_now, ready, all_blocks)
        last = stratum + 1 == stratum_total
        if last:
            step_mask = stratum_masks[stratum]
        else:
            step_mask = jnp.bitwise_xor(stratum_masks[stratum], stratum_masks[stratum + 1])

        def user_step(grad_user=grad_user, user_rows=user_rows, last=last, stratum=stratum):
            grad_total = item_sum(grad_user)
            rows = user_rows - LEARNING_RATE * (grad_total + WEIGHT_DECAY * user_rows)
            return rows, (None if last else tables(stratum + 1))

        panel_now, (user_rows, ready) = moved(panel_next, step_mask, user_step, not last)
    return (user_rows, panel_now)


def solution(mesh):
    placed = (
        P(("groups", "user"), None),
        P(("groups", "user", "item"), None),
        P("groups"),
        P(("groups", "user"), "item", None),
        P(("groups", "user"), "item", None),
        P(("groups", "user"), "item", None, None, None),
    )
    return jax.shard_map(
        local,
        mesh=mesh,
        in_specs=placed,
        out_specs=(P(("groups", "user"), None), P(("groups", "user", "item"), None)),
        check_vma=False,
    )
```

```python
import functools

import jax
import jax.numpy as jnp
from jax import lax
from jax.experimental import pallas as pl
from jax.experimental.pallas import tpu as pltpu
from jax.sharding import PartitionSpec as P

LEARNING_RATE = 0.02
WEIGHT_DECAY = 0.1
TILES_PER_STEP = 8


def moved(value, partner_mask, work, may_stay):
    count = lax.axis_size("user")

    def branch(mask):
        def run(held):
            done = work()
            if mask == 0:
                return held, done
            pairs = [(source, source ^ mask) for source in range(count)]
            return lax.optimization_barrier((lax.ppermute(held, "user", pairs), done))

        return run

    if may_stay:
        return lax.switch(partner_mask, [branch(mask) for mask in range(count)], value)
    return lax.switch(partner_mask - 1, [branch(mask) for mask in range(1, count)], value)


def item_sum(value):
    if lax.axis_size("item") == 2:
        return value + lax.ppermute(value, "item", [(0, 1), (1, 0)])
    return lax.psum(value, "item")


def grads_kernel(item_tiles, slot_ref, live_ref, user_ref, panel_ref, *rest):
    block_refs = rest[: TILES_PER_STEP * item_tiles]
    grad_user_ref, panel_next_ref, panel_bf_ref, grad_panel_ref = rest[TILES_PER_STEP * item_tiles :]
    step = pl.program_id(0)
    tile_size = block_refs[0].shape[-1]

    @pl.when(step == 0)
    def _():
        grad_panel_ref[...] = jnp.zeros_like(grad_panel_ref)
        panel_bf_ref[...] = panel_ref[...].astype(jnp.bfloat16)

    user_bf = user_ref[...].astype(jnp.bfloat16)
    panel_bf = panel_bf_ref[...]
    scores = lax.dot_general(
        user_bf, panel_bf, (((1,), (1,)), ((), ())), preferred_element_type=jnp.float32
    )
    pieces = []
    for inner in range(TILES_PER_STEP):
        row = []
        for column in range(item_tiles):
            code = (step * TILES_PER_STEP + inner) * item_tiles + column
            live = live_ref[code].astype(jnp.float32)
            block = block_refs[inner * item_tiles + column][...].astype(jnp.float32)
            part = scores[inner * tile_size : (inner + 1) * tile_size, column * tile_size : (column + 1) * tile_size]
            row.append(((part - block) * live).astype(jnp.bfloat16))
        pieces.append(jnp.concatenate(row, axis=1))
    errors = jnp.concatenate(pieces, axis=0)
    grad_user_ref[...] = jnp.dot(errors, panel_bf, preferred_element_type=jnp.float32)
    grad_panel_ref[...] += lax.dot_general(
        errors, user_bf, (((0,), (0,)), ((), ())), preferred_element_type=jnp.float32
    )

    @pl.when(step == pl.num_programs(0) - 1)
    def _():
        panel = panel_ref[...]
        panel_next_ref[...] = panel - LEARNING_RATE * (grad_panel_ref[...] + WEIGHT_DECAY * panel)


def slot_tables(codes, count, first, code_count, per_step):
    slot_count = codes.shape[0]
    hits = (codes[:, None] == lax.iota(jnp.int32, code_count)[None, :]) & (
        lax.iota(jnp.int32, slot_count) < count
    )[:, None]
    live = jnp.any(hits, axis=0)
    slot_of = first + jnp.sum(jnp.where(hits, lax.iota(jnp.int32, slot_count)[:, None], 0), axis=0)
    steps = code_count // per_step
    live_steps = live.reshape(steps, per_step)
    slots = slot_of.reshape(steps, per_step)
    later = [None] * steps
    later[-1] = jnp.where(live_steps[-1], slots[-1], first)
    for step in range(steps - 2, -1, -1):
        later[step] = jnp.where(live_steps[step], slots[step], later[step + 1])
    filled = [later[0]]
    for step in range(1, steps):
        filled.append(jnp.where(live_steps[step], slots[step], filled[-1]))
    return jnp.concatenate(filled), live.astype(jnp.int32)


def local_grads(user_rows, panel_bf, tables, blocks):
    slot_of, live = tables
    tile_size = blocks.shape[-1]
    rank = user_rows.shape[1]
    user_tiles = user_rows.shape[0] // tile_size
    item_tiles = panel_bf.shape[0] // tile_size
    code_count = user_tiles * item_tiles

    def block_spec(inner, column):
        def index(step, slot_ref, live_ref):
            return (slot_ref[(step * TILES_PER_STEP + inner) * item_tiles + column], 0, 0)

        return pl.BlockSpec((None, tile_size, tile_size), index)

    rows = TILES_PER_STEP * tile_size
    columns = item_tiles * tile_size
    grid_spec = pltpu.PrefetchScalarGridSpec(
        num_scalar_prefetch=2,
        grid=(user_tiles // TILES_PER_STEP,),
        in_specs=[
            pl.BlockSpec((rows, rank), lambda step, slot_ref, live_ref: (step, 0)),
            pl.BlockSpec((columns, rank), lambda step, slot_ref, live_ref: (0, 0)),
        ]
        + [block_spec(inner, column) for inner in range(TILES_PER_STEP) for column in range(item_tiles)],
        out_specs=[
            pl.BlockSpec((rows, rank), lambda step, slot_ref, live_ref: (step, 0)),
            pl.BlockSpec((columns, rank), lambda step, slot_ref, live_ref: (0, 0)),
        ],
        scratch_shapes=[pltpu.VMEM((columns, rank), jnp.bfloat16), pltpu.VMEM((columns, rank), jnp.float32)],
    )
    flops = 3 * 2 * code_count * tile_size * tile_size * rank
    moved_bytes = user_rows.size * 8 + panel_bf.size * 8 + code_count * tile_size * tile_size * 2
    return pl.pallas_call(
        functools.partial(grads_kernel, item_tiles),
        grid_spec=grid_spec,
        out_shape=[
            jax.ShapeDtypeStruct(user_rows.shape, jnp.float32),
            jax.ShapeDtypeStruct(panel_bf.shape, jnp.float32),
        ],
        compiler_params=pltpu.CompilerParams(dimension_semantics=("arbitrary",)),
        cost_estimate=pl.CostEstimate(flops=flops, bytes_accessed=moved_bytes, transcendentals=0),
    )(slot_of, live, user_rows, panel_bf, *([blocks] * (TILES_PER_STEP * item_tiles)))


def local(user_factors, item_factors, stratum_masks, block_codes, block_counts, ratings):
    stratum_total = stratum_masks.shape[0]
    slot_count = block_codes.shape[-1] // stratum_total
    tile_size = ratings.shape[-1]
    code_count = (user_factors.shape[0] // tile_size) * (item_factors.shape[0] // tile_size)
    all_blocks = ratings.reshape(-1, tile_size, tile_size)

    def tables(stratum):
        codes = block_codes[0, 0, stratum * slot_count : (stratum + 1) * slot_count]
        count = block_counts[0, 0, stratum]
        per_step = TILES_PER_STEP * (item_factors.shape[0] // tile_size)
        return slot_tables(codes, count, stratum * slot_count, code_count, per_step)

    user_rows = user_factors
    panel_now, ready = moved(item_factors, stratum_masks[0], lambda: tables(0), False)
    for stratum in range(stratum_total):
        grad_user, panel_next = local_grads(user_rows, panel_now, ready, all_blocks)
        last = stratum + 1 == stratum_total
        if last:
            step_mask = stratum_masks[stratum]
        else:
            step_mask = jnp.bitwise_xor(stratum_masks[stratum], stratum_masks[stratum + 1])

        def user_step(grad_user=grad_user, user_rows=user_rows, last=last, stratum=stratum):
            grad_total = item_sum(grad_user)
            rows = user_rows - LEARNING_RATE * (grad_total + WEIGHT_DECAY * user_rows)
            return rows, (None if last else tables(stratum + 1))

        panel_now, (user_rows, ready) = moved(panel_next, step_mask, user_step, not last)
    return (user_rows, panel_now)


def solution(mesh):
    placed = (
        P(("groups", "user"), None),
        P(("groups", "user", "item"), None),
        P("groups"),
        P(("groups", "user"), "item", None),
        P(("groups", "user"), "item", None),
        P(("groups", "user"), "item", None, None, None),
    )
    return jax.shard_map(
        local,
        mesh=mesh,
        in_specs=placed,
        out_specs=(P(("groups", "user"), None), P(("groups", "user", "item"), None)),
        check_vma=False,
    )
```
